32 devices in a mesh: segment: 2 (over core), expert: 16 (over z, y, x).
Axes of the slice: x: 2, y: 2, z: 4, core: 2. Of those that a mesh axis runs over, the one named last changes fastest.
Arguments:
- hidden_in: bfloat16 [2, 256, 7168], P('segment', 'expert'), may hold values from -6 to 6
- norm_gain: bfloat16 [2, 7168], P('segment'), may hold values from 0.25 to 1.75
- up_proj: bfloat16 [2, 8192, 7168], P('segment', 'expert'), may hold values from -0.0625 to 0.0625
- down_proj: bfloat16 [2, 8192, 7168], P('segment', 'expert'), may hold values from -0.1875 to 0.1875
- expert_ids: int32 [2, 256, 2], P('segment', 'expert'), may hold values from 0 to 7, all different within a row; in each aligned block of 16 rows (0 to 15, 16 to 31, ..., all dimensions but the last counted through in order) at most 7 rows name the same one
- gate_weights: float32 [2, 256, 2], P('segment', 'expert'), may hold values from 0.2 to 1
Outputs:
- handed_on: bfloat16 [2, 256, 7168], P('segment', 'expert')
The draws below stay inside these ranges and needn't reach their ends.
Inputs may be any that keep to these rules, and one draw needn't show every extreme that they name: `expert_ids`: each row names 2 different experts. Among the rows of one device in one section no expert is named by more than 7 rows, and in some device an expert is named by exactly 7.
All inputs are finite; a program needn't handle non-finite values.
Results may differ from the reference program's by a relative error of at most 0.0075.
Values may be sent and summed in bfloat16 or wider, within the bound.
No kernel may reach another device: no remote copies, remote signals or barrier semaphores. Data moves between devices by JAX's collectives and lax.ppermute only.
A program may use at most 64 MiB of HBM per device.

```python
import math
import jax
import jax.numpy as jnp
import numpy as np
from jax import lax

D = 7168
FF_E = 1024
EXPERTS = 8
TOP = 2
ROWS_DEV = 16
CAP = 7
BPE = 2
FB = 512
ROWS = 256
SEGMENTS = 2
N_EXPERT = 16


def shard_levels(key, extent, pieces, least, largest):
    level = 1.0
    for position, shards_of in pieces:
        heights = jax.random.uniform(jax.random.fold_in(jax.random.fold_in(key, 6), position), (shards_of,), jnp.float32, least / len(pieces), largest / len(pieces))
        level = level * jnp.repeat(jnp.exp(heights), extent[position] // shards_of).reshape((-1,) + (1,) * (len(extent) - 1 - position))
    return level


def shared_out(own_key, own, number, rows, number_of, top, most, slope):
    sequence = jax.random.permutation(own_key, number_of)
    crowded, common = load_shares(number_of, rows * top, most, slope, True), load_shares(number_of, rows * top, most, slope, False)
    places = jnp.arange(number_of)

    def named(tallies, offset_by):
        used = int((tallies > 0).sum())
        fixed = max(1, used // 4)
        passed = fixed + (places - fixed + offset_by * (used - fixed)) % max(1, number_of - fixed)
        return jnp.zeros((number_of,), jnp.int32).at[sequence[jnp.where(places < fixed, places, passed)]].set(jnp.asarray(tallies, jnp.int32))

    tallies = jnp.where(number % 4 == 0, named(crowded, number // 4), named(common, number - number // 4 - 1))
    mixed = jax.random.permutation(jax.random.fold_in(own, 3), number_of)
    giver, receiver = mixed[0:number_of // 2 * 2:2], mixed[1:number_of // 2 * 2:2]
    slack = jnp.minimum(tallies[giver] - 1, most - tallies[receiver]) // 2
    slack = jnp.where((giver == sequence[0]) | (receiver == sequence[0]) | (tallies[receiver] == 0), 0, jnp.maximum(slack, 0))
    passed = jax.random.randint(jax.random.fold_in(own, 4), (number_of // 2,), 0, 1 << 20) % (slack + 1)
    tallies = tallies.at[giver].add(-passed).at[receiver].add(passed)
    labels = jnp.searchsorted(jnp.cumsum(tallies), jnp.arange(rows * top), side="right").astype(jnp.int32)
    grid = labels.reshape(top, rows).T
    grid = grid[jax.random.permutation(jax.random.fold_in(own, 1), rows)]
    offset_by = jax.random.randint(jax.random.fold_in(own, 2), (rows, 1), 0, top)
    return jnp.take_along_axis(grid, (jnp.arange(top)[None, :] + offset_by) % top, axis=1)


def load_shares(count, total, limit, lean, full):
    loads = [(1 << 20) // math.isqrt(grade ** lean) + 1 for grade in range(1, count + 1)]
    largest = limit if full else min(limit, max(-(-total // count), total * loads[0] // sum(loads)))
    least = 1 if total - largest >= count - 1 else 0
    counts, rest = [largest] + [least] * (count - 1), total - largest - least * (count - 1)
    while rest > 0:
        free = [i for i in range(1, count) if counts[i] < largest] or [i for i in range(1, count) if counts[i] < limit]
        mass, left = sum([loads[i] for i in free]), rest
        for i in free:
            addition = min(limit - counts[i], max(1, left * loads[i] // mass), rest)
            counts[i] = counts[i] + addition
            rest = rest - addition
    return np.array(counts)


def normal_values(rng, shape, width, reach, pieces=(), kind=jnp.bfloat16):
    drawn = jax.random.normal(rng, shape, jnp.float32) * width
    if len(pieces) > 0:
        drawn = shard_levels(rng, shape, pieces, -0.22, 0.18) * drawn
    return jnp.clip(drawn, min=-reach, max=reach).astype(kind)


def setup_inputs(seed: int = 0) -> dict:
    streams_of = jax.random.split(jax.random.key(seed), 7)
    hidden_in = normal_values(streams_of[0], (SEGMENTS, ROWS, D), 1.0, 6.0, ((0, 2), (1, 16)))
    norm_gain = jnp.clip(1.0 + 0.15 * jax.random.normal(streams_of[1], (SEGMENTS, D), jnp.float32), 0.25, 1.75).astype(jnp.bfloat16)
    up_proj = normal_values(streams_of[2], (SEGMENTS, EXPERTS * FF_E, D), D ** -0.5, 0.0625, ((0, 2), (1, 16)))
    down_proj = normal_values(streams_of[3], (SEGMENTS, EXPERTS * FF_E, D), FF_E ** -0.5, 0.1875, ((0, 2), (1, 16)))
    expert_ids_keys = jax.random.split(jax.random.fold_in(streams_of[4], 1), SEGMENTS * ROWS // ROWS_DEV)
    expert_ids_turns = jax.random.permutation(jax.random.fold_in(streams_of[4], 3), SEGMENTS * ROWS // ROWS_DEV)
    expert_ids = jax.vmap(lambda own, number: shared_out(jax.random.fold_in(streams_of[4], 2), own, number, ROWS_DEV, EXPERTS, TOP, CAP, 2))(expert_ids_keys, expert_ids_turns).reshape((SEGMENTS, ROWS, TOP))
    gate_weights = jnp.clip(0.2 + 0.8 * jax.random.uniform(streams_of[5], (SEGMENTS, ROWS, TOP), jnp.float32) ** shard_levels(streams_of[5], (SEGMENTS, ROWS, TOP), ((0, 2), (1, 16)), -0.2, 0.2), 0.2, 1.0)
    return {"hidden_in": hidden_in, "norm_gain": norm_gain, "up_proj": up_proj, "down_proj": down_proj, "expert_ids": expert_ids, "gate_weights": gate_weights}


def one_section(tokens, gain, up_rows, down_rows, routes, weights):
    square = lax.optimization_barrier(jnp.mean(tokens.astype(jnp.float32) ** 2, axis=-1, keepdims=True))
    normed = (tokens.astype(jnp.float32) * lax.rsqrt(square + 1e-06) * gain.astype(jnp.float32)).astype(jnp.bfloat16)
    flat_ids = routes.reshape(-1)
    flat_weights = weights.reshape(-1)
    owner_rows = (jnp.arange(ROWS * TOP) // TOP).astype(jnp.int32)
    slots = N_EXPERT * CAP

    def per_expert(total, expert):
        chosen = flat_ids == expert
        picked = jnp.nonzero(chosen, size=slots, fill_value=0)[0].astype(jnp.int32)
        valid = jnp.arange(slots) < jnp.sum(chosen.astype(jnp.int32))
        row_index = owner_rows[picked]
        inputs = normed[row_index]
        start = (expert * FF_E).astype(jnp.int32)
        up_expert = lax.dynamic_slice_in_dim(up_rows, start, FF_E, 0)
        down_expert = lax.dynamic_slice_in_dim(down_rows, start, FF_E, 0)
        inner = jnp.dot(inputs, up_expert.T, preferred_element_type=jnp.float32)
        active = jax.nn.silu(inner).astype(jnp.bfloat16)
        blocks = jnp.einsum('nbf,bfd->nbd', active.reshape(slots, BPE, FB).astype(jnp.float32), down_expert.reshape(BPE, FB, D).astype(jnp.float32), precision=lax.Precision.HIGHEST)
        summed = lax.optimization_barrier(jnp.sum(blocks.astype(jnp.bfloat16).astype(jnp.float32), axis=1))
        scale = jnp.where(valid, flat_weights[picked], jnp.float32(0.0))
        total = total.at[row_index].add(scale[:, None] * summed)
        return (total, None)
    mixed, unused = lax.scan(per_expert, jnp.zeros((ROWS, D), jnp.float32), jnp.arange(EXPERTS).astype(jnp.int32))
    return (tokens.astype(jnp.float32) + mixed).astype(jnp.bfloat16)

def reference(hidden_in, norm_gain, up_proj, down_proj, expert_ids, gate_weights):
    results = []
    for section in range(SEGMENTS):
        results.append(one_section(hidden_in[section], norm_gain[section], up_proj[section], down_proj[section], expert_ids[section], gate_weights[section]))
    stacked = jnp.stack(results, axis=0)
    return jnp.roll(stacked, 1, axis=0)
```

```python
import jax
import jax.numpy as jnp
from jax import lax
from jax.sharding import PartitionSpec as P

EXPERTS = 8


def passed_along(shard, axis, by):
    count = lax.axis_size(axis)
    return lax.ppermute(shard, axis, [(i, (i + by) % count) for i in range(count)])


def shards(hidden_in, norm_gain, up_proj, down_proj, expert_ids, gate_weights):
    members = lax.axis_size("expert")
    me = lax.axis_index("expert")
    tokens = hidden_in[0]
    gain = norm_gain[0]
    up_block = up_proj[0]
    down_block = down_proj[0]
    local_units = up_block.shape[0]
    units_per_expert = local_units * members // EXPERTS
    my_expert = (me * local_units) // units_per_expert
    square = jnp.mean(tokens.astype(jnp.float32) ** 2, axis=-1, keepdims=True)
    normed = (
        tokens.astype(jnp.float32) * lax.rsqrt(square + 1e-06) * gain.astype(jnp.float32)
    ).astype(jnp.bfloat16)
    all_rows = lax.all_gather(normed, "expert", axis=0, tiled=True)
    all_ids = lax.all_gather(expert_ids[0], "expert", axis=0, tiled=True)
    all_gates = lax.all_gather(gate_weights[0], "expert", axis=0, tiled=True)
    scale = jnp.sum(jnp.where(all_ids == my_expert, all_gates, 0.0), axis=-1, keepdims=True)
    inner = jnp.einsum("rd,fd->rf", all_rows, up_block, preferred_element_type=jnp.float32)
    active = jax.nn.silu(inner).astype(jnp.bfloat16)
    partial = jnp.dot(active, down_block, preferred_element_type=jnp.float32).astype(jnp.bfloat16)
    contribution = partial.astype(jnp.float32) * scale
    mixture = lax.psum_scatter(contribution, "expert", scatter_dimension=0, tiled=True)
    section_out = (tokens.astype(jnp.float32) + mixture).astype(jnp.bfloat16)
    handed = passed_along(section_out, "segment", 1)
    return handed[None]


def solution(mesh):
    in_specs = (
        P("segment", "expert", None),
        P("segment", None),
        P("segment", "expert", None),
        P("segment", "expert", None),
        P("segment", "expert", None),
        P("segment", "expert", None),
    )
    out_specs = P("segment", "expert", None)
    return jax.shard_map(shards, mesh=mesh, in_specs=in_specs, out_specs=out_specs, check_vma=False)
```

```python
import jax
import jax.numpy as jnp
from jax import lax
from jax.sharding import PartitionSpec as P

EXPERTS = 8
CAP = 7


def passed_along(shard, axis, by):
    count = lax.axis_size(axis)
    return lax.ppermute(shard, axis, [(i, (i + by) % count) for i in range(count)])


def shards(hidden_in, norm_gain, up_proj, down_proj, expert_ids, gate_weights):
    members = lax.axis_size("expert")
    per_group = members // EXPERTS
    tokens = hidden_in[0]
    gain = norm_gain[0]
    up_block = up_proj[0]
    down_block = down_proj[0]
    routes = expert_ids[0]
    weights = gate_weights[0]
    rows_here, width = tokens.shape
    top = routes.shape[1]
    square = jnp.mean(tokens.astype(jnp.float32) ** 2, axis=-1, keepdims=True)
    normed = (
        tokens.astype(jnp.float32) * lax.rsqrt(square + 1e-06) * gain.astype(jnp.float32)
    ).astype(jnp.bfloat16)
    flat = routes.reshape(-1)
    onehot = (flat[:, None] == jnp.arange(EXPERTS)[None, :]).astype(jnp.int32)
    positions = jnp.arange(flat.shape[0])
    earlier = (positions[None, :] < positions[:, None]).astype(jnp.int32)
    rank = jnp.sum(jnp.dot(earlier, onehot, preferred_element_type=jnp.int32) * onehot, axis=1)
    rank = rank.reshape(rows_here, top)
    slot = jnp.arange(members * CAP)
    slot_device = slot // CAP
    slot_rank = slot % CAP
    slot_expert = slot_device // per_group
    hits = (routes[None, :, :] == slot_expert[:, None, None]) & (rank[None, :, :] == slot_rank[:, None, None])
    picker = jnp.any(hits, axis=2).astype(jnp.bfloat16)
    outgoing = jnp.dot(picker, normed, preferred_element_type=jnp.float32).astype(jnp.bfloat16)
    outgoing = outgoing.reshape(members, CAP, width)
    incoming = lax.all_to_all(outgoing, "expert", split_axis=0, concat_axis=0, tiled=True)
    inner = jnp.einsum("spd,fd->spf", incoming, up_block, preferred_element_type=jnp.float32)
    active = jax.nn.silu(inner).astype(jnp.bfloat16)
    partial = jnp.einsum("spf,fd->spd", active, down_block, preferred_element_type=jnp.float32).astype(jnp.bfloat16)
    returned = lax.all_to_all(partial, "expert", split_axis=0, concat_axis=0, tiled=True)
    combine = jnp.sum(jnp.where(hits, weights[None, :, :], 0.0), axis=2).T.reshape(rows_here, members, CAP)
    mixture = jnp.einsum("rsp,spd->rd", combine, returned.astype(jnp.float32), precision=lax.Precision.HIGHEST)
    section_out = (tokens.astype(jnp.float32) + mixture).astype(jnp.bfloat16)
    handed = passed_along(section_out, "segment", 1)
    return handed[None]


def solution(mesh):
    in_specs = (
        P("segment", "expert", None),
        P("segment", None),
        P("segment", "expert", None),
        P("segment", "expert", None),
        P("segment", "expert", None),
        P("segment", "expert", None),
    )
    out_specs = P("segment", "expert", None)
    return jax.shard_map(shards, mesh=mesh, in_specs=in_specs, out_specs=out_specs, check_vma=False)
```

```python
import jax
import jax.numpy as jnp
from jax import lax
from jax.sharding import PartitionSpec as P

EXPERTS = 8
CAP = 7


def passed_along(shard, axis, by):
    count = lax.axis_size(axis)
    return lax.ppermute(shard, axis, [(i, (i + by) % count) for i in range(count)])


def shards(hidden_in, norm_gain, up_proj, down_proj, expert_ids, gate_weights):
    members = lax.axis_size("expert")
    per_group = members // EXPERTS
    tokens = hidden_in[0]
    gain = norm_gain[0]
    up_block = up_proj[0]
    down_block = down_proj[0]
    routes = expert_ids[0]
    weights = gate_weights[0]
    rows_here, width = tokens.shape
    top = routes.shape[1]
    square = jnp.mean(tokens.astype(jnp.float32) ** 2, axis=-1, keepdims=True)
    normed = (
        tokens.astype(jnp.float32) * lax.rsqrt(square + 1e-06) * gain.astype(jnp.float32)
    ).astype(jnp.bfloat16)
    flat = routes.reshape(-1)
    onehot = (flat[:, None] == jnp.arange(EXPERTS)[None, :]).astype(jnp.int32)
    positions = jnp.arange(flat.shape[0])
    earlier = (positions[None, :] < positions[:, None]).astype(jnp.int32)
    rank = jnp.sum(jnp.dot(earlier, onehot, preferred_element_type=jnp.int32) * onehot, axis=1)
    rank = rank.reshape(rows_here, top)
    slot = jnp.arange(members * CAP)
    slot_device = slot % members
    slot_rank = slot // members
    slot_expert = slot_device // per_group
    hits = (routes[None, :, :] == slot_expert[:, None, None]) & (rank[None, :, :] == slot_rank[:, None, None])
    picker = jnp.any(hits, axis=2).astype(jnp.bfloat16)
    outgoing = jnp.dot(picker, normed, preferred_element_type=jnp.float32).astype(jnp.bfloat16)
    outgoing = outgoing.reshape(CAP, members, width)
    incoming = lax.all_to_all(outgoing, "expert", split_axis=1, concat_axis=1, tiled=True)
    inner = jnp.einsum("psd,fd->psf", incoming, up_block, preferred_element_type=jnp.float32)
    active = jax.nn.silu(inner).astype(jnp.bfloat16)
    partial = jnp.einsum("psf,fd->psd", active, down_block, preferred_element_type=jnp.float32).astype(jnp.bfloat16)
    returned = lax.all_to_all(partial, "expert", split_axis=1, concat_axis=1, tiled=True)
    combine = jnp.sum(jnp.where(hits, weights[None, :, :], 0.0), axis=2).T.reshape(rows_here, CAP, members)
    mixture = jnp.einsum("rps,psd->rd", combine, returned.astype(jnp.float32), precision=lax.Precision.HIGHEST)
    section_out = (tokens.astype(jnp.float32) + mixture).astype(jnp.bfloat16)
    handed = passed_along(section_out, "segment", 1)
    return handed[None]


def solution(mesh):
    in_specs = (
        P("segment", "expert", None),
        P("segment", None),
        P("segment", "expert", None),
        P("segment", "expert", None),
        P("segment", "expert", None),
        P("segment", "expert", None),
    )
    out_specs = P("segment", "expert", None)
    return jax.shard_map(shards, mesh=mesh, in_specs=in_specs, out_specs=out_specs, check_vma=False)
```

```python
import jax
import jax.numpy as jnp
from jax import lax
from jax.sharding import PartitionSpec as P

EXPERTS = 8
CAP = 7


def passed_along(shard, axis, by):
    count = lax.axis_size(axis)
    return lax.ppermute(shard, axis, [(i, (i + by) % count) for i in range(count)])


def shards(hidden_in, norm_gain, up_proj, down_proj, expert_ids, gate_weights):
    members = lax.axis_size("expert")
    per_group = members // EXPERTS
    tokens = hidden_in[0]
    gain = norm_gain[0]
    up_block = up_proj[0]
    down_block = down_proj[0]
    routes = expert_ids[0]
    weights = gate_weights[0]
    rows_here, width = tokens.shape
    top = routes.shape[1]
    square = jnp.mean(tokens.astype(jnp.float32) ** 2, axis=-1, keepdims=True)
    normed = (
        tokens.astype(jnp.float32) * lax.rsqrt(square + 1e-06) * gain.astype(jnp.float32)
    ).astype(jnp.bfloat16)
    flat = routes.reshape(-1)
    onehot = (flat[:, None] == jnp.arange(EXPERTS)[None, :]).astype(jnp.int32)
    positions = jnp.arange(flat.shape[0])
    earlier = (positions[None, :] < positions[:, None]).astype(jnp.int32)
    rank = jnp.sum(jnp.dot(earlier, onehot, preferred_element_type=jnp.int32) * onehot, axis=1)
    rank = rank.reshape(rows_here, top)
    slot = jnp.arange(members * CAP)
    slot_device = slot % members
    slot_rank = slot // members
    slot_expert = slot_device // per_group
    hits = (routes[None, :, :] == slot_expert[:, None, None]) & (rank[None, :, :] == slot_rank[:, None, None])
    picker = jnp.any(hits, axis=2).astype(jnp.bfloat16)
    outgoing = jnp.dot(picker, normed, preferred_element_type=jnp.float32).astype(jnp.bfloat16)
    outgoing = outgoing.reshape(CAP, members, width)
    incoming = lax.all_to_all(outgoing, "expert", split_axis=1, concat_axis=1, tiled=True)
    inner = jnp.einsum("psd,fd->psf", incoming, up_block, preferred_element_type=jnp.float32)
    active = jax.nn.silu(inner).astype(jnp.bfloat16)
    partial = jnp.einsum("psf,fd->psd", active, down_block, preferred_element_type=jnp.float32).astype(jnp.bfloat16)
    returned = lax.all_to_all(partial, "expert", split_axis=1, concat_axis=1, tiled=True)
    combine = jnp.sum(jnp.where(hits, weights[None, :, :], 0.0), axis=2).T.reshape(rows_here, CAP, members)
    combine_hi = combine.astype(jnp.bfloat16)
    combine_lo = (combine - combine_hi.astype(jnp.float32)).astype(jnp.bfloat16)
    mixture = jnp.einsum("rps,psd->rd", combine_hi, returned, preferred_element_type=jnp.float32)
    mixture = mixture + jnp.einsum("rps,psd->rd", combine_lo, returned, preferred_element_type=jnp.float32)
    section_out = (tokens.astype(jnp.float32) + mixture).astype(jnp.bfloat16)
    handed = passed_along(section_out, "segment", 1)
    return handed[None]


def solution(mesh):
    in_specs = (
        P("segment", "expert", None),
        P("segment", None),
        P("segment", "expert", None),
        P("segment", "expert", None),
        P("segment", "expert", None),
        P("segment", "expert", None),
    )
    out_specs = P("segment", "expert", None)
    return jax.shard_map(shards, mesh=mesh, in_specs=in_specs, out_specs=out_specs, check_vma=False)
```

```python
import jax
import jax.numpy as jnp
from jax import lax
from jax.sharding import PartitionSpec as P

EXPERTS = 8
CAP = 7


def passed_along(shard, axis, by):
    count = lax.axis_size(axis)
    return lax.ppermute(shard, axis, [(i, (i + by) % count) for i in range(count)])


def shards(hidden_in, norm_gain, up_proj, down_proj, expert_ids, gate_weights):
    members = lax.axis_size("expert")
    per_group = members // EXPERTS
    tokens = hidden_in[0]
    gain = norm_gain[0]
    up_block = up_proj[0]
    down_block = down_proj[0]
    routes = expert_ids[0]
    weights = gate_weights[0]
    rows_here, width = tokens.shape
    top = routes.shape[1]
    square = jnp.mean(tokens.astype(jnp.float32) ** 2, axis=-1, keepdims=True)
    normed = (
        tokens.astype(jnp.float32) * lax.rsqrt(square + 1e-06) * gain.astype(jnp.float32)
    ).astype(jnp.bfloat16)
    flat = routes.reshape(-1)
    onehot = (flat[:, None] == jnp.arange(EXPERTS)[None, :]).astype(jnp.int32)
    positions = jnp.arange(flat.shape[0])
    earlier = (positions[None, :] < positions[:, None]).astype(jnp.int32)
    rank = jnp.sum(jnp.dot(earlier, onehot, preferred_element_type=jnp.int32) * onehot, axis=1)
    rank = rank.reshape(rows_here, top)
    slot = jnp.arange(members * CAP)
    slot_device = slot % members
    slot_rank = slot // members
    slot_expert = slot_device // per_group
    hits = (routes[None, :, :] == slot_expert[:, None, None]) & (rank[None, :, :] == slot_rank[:, None, None])
    picker = jnp.any(hits, axis=2).astype(jnp.bfloat16)
    outgoing = jnp.dot(picker, normed, preferred_element_type=jnp.float32).astype(jnp.bfloat16)
    outgoing = outgoing.reshape(CAP, members, width)
    incoming = lax.all_to_all(outgoing, "expert", split_axis=1, concat_axis=1, tiled=True)
    combine = jnp.sum(jnp.where(hits, weights[None, :, :], 0.0), axis=2).T.reshape(rows_here, CAP, members)
    incoming, combine = lax.optimization_barrier((incoming, combine))
    inner = jnp.einsum("psd,fd->psf", incoming, up_block, preferred_element_type=jnp.float32)
    active = jax.nn.silu(inner).astype(jnp.bfloat16)
    partial = jnp.einsum("psf,fd->psd", active, down_block, preferred_element_type=jnp.float32).astype(jnp.bfloat16)
    returned = lax.all_to_all(partial, "expert", split_axis=1, concat_axis=1, tiled=True)
    combine_hi = combine.astype(jnp.bfloat16)
    combine_lo = (combine - combine_hi.astype(jnp.float32)).astype(jnp.bfloat16)
    mixture = jnp.einsum("rps,psd->rd", combine_hi, returned, preferred_element_type=jnp.float32)
    mixture = mixture + jnp.einsum("rps,psd->rd", combine_lo, returned, preferred_element_type=jnp.float32)
    section_out = (tokens.astype(jnp.float32) + mixture).astype(jnp.bfloat16)
    handed = passed_along(section_out, "segment", 1)
    return handed[None]


def solution(mesh):
    in_specs = (
        P("segment", "expert", None),
        P("segment", None),
        P("segment", "expert", None),
        P("segment", "expert", None),
        P("segment", "expert", None),
        P("segment", "expert", None),
    )
    out_specs = P("segment", "expert", None)
    return jax.shard_map(shards, mesh=mesh, in_specs=in_specs, out_specs=out_specs, check_vma=False)
```

```python
import jax
import jax.numpy as jnp
from jax import lax
from jax.sharding import PartitionSpec as P

EXPERTS = 8
CAP = 7


def passed_along(shard, axis, by):
    count = lax.axis_size(axis)
    return lax.ppermute(shard, axis, [(i, (i + by) % count) for i in range(count)])


def shards(hidden_in, norm_gain, up_proj, down_proj, expert_ids, gate_weights):
    members = lax.axis_size("expert")
    per_group = members // EXPERTS
    tokens = hidden_in[0]
    gain = norm_gain[0]
    up_block = up_proj[0]
    down_block = down_proj[0]
    routes = expert_ids[0]
    weights = gate_weights[0]
    rows_here, width = tokens.shape
    top = routes.shape[1]
    square = jnp.mean(tokens.astype(jnp.float32) ** 2, axis=-1, keepdims=True)
    normed = (
        tokens.astype(jnp.float32) * lax.rsqrt(square + 1e-06) * gain.astype(jnp.float32)
    ).astype(jnp.bfloat16)
    chosen = routes[:, :, None] == jnp.arange(EXPERTS)[None, None, :]
    named = jnp.sum(chosen.astype(jnp.int32), axis=1)
    positions = jnp.arange(rows_here)
    earlier = (positions[None, :] < positions[:, None]).astype(jnp.int32)
    before = jnp.dot(earlier, named, preferred_element_type=jnp.int32)
    rank = jnp.sum(jnp.where(chosen, before[:, None, :], 0), axis=2)
    slot = jnp.arange(members * CAP)
    slot_device = slot % members
    slot_rank = slot // members
    slot_expert = slot_device // per_group
    hits = (routes[None, :, :] == slot_expert[:, None, None]) & (rank[None, :, :] == slot_rank[:, None, None])
    picker = jnp.any(hits, axis=2).astype(jnp.bfloat16)
    outgoing = jnp.dot(picker, normed, preferred_element_type=jnp.float32).astype(jnp.bfloat16)
    outgoing = outgoing.reshape(CAP, members, width)
    incoming = lax.all_to_all(outgoing, "expert", split_axis=1, concat_axis=1, tiled=True)
    inner = jnp.einsum("psd,fd->psf", incoming, up_block, preferred_element_type=jnp.float32)
    active = jax.nn.silu(inner).astype(jnp.bfloat16)
    partial = jnp.einsum("psf,fd->psd", active, down_block, preferred_element_type=jnp.float32).astype(jnp.bfloat16)
    returned = lax.all_to_all(partial, "expert", split_axis=1, concat_axis=1, tiled=True)
    combine = jnp.sum(jnp.where(hits, weights[None, :, :], 0.0), axis=2).T.reshape(rows_here, CAP, members)
    combine_hi = combine.astype(jnp.bfloat16)
    combine_lo = (combine - combine_hi.astype(jnp.float32)).astype(jnp.bfloat16)
    mixture = jnp.einsum("rps,psd->rd", combine_hi, returned, preferred_element_type=jnp.float32)
    mixture = mixture + jnp.einsum("rps,psd->rd", combine_lo, returned, preferred_element_type=jnp.float32)
    section_out = (tokens.astype(jnp.float32) + mixture).astype(jnp.bfloat16)
    handed = passed_along(section_out, "segment", 1)
    return handed[None]


def solution(mesh):
    in_specs = (
        P("segment", "expert", None),
        P("segment", None),
        P("segment", "expert", None),
        P("segment", "expert", None),
        P("segment", "expert", None),
        P("segment", "expert", None),
    )
    out_specs = P("segment", "expert", None)
    return jax.shard_map(shards, mesh=mesh, in_specs=in_specs, out_specs=out_specs, check_vma=False)
```

```python
import jax
import jax.numpy as jnp
from jax import lax
from jax.sharding import PartitionSpec as P

EXPERTS = 8
CAP = 7
LANES = 128


def passed_along(shard, axis, by):
    count = lax.axis_size(axis)
    return lax.ppermute(shard, axis, [(i, (i + by) % count) for i in range(count)])


def shards(hidden_in, norm_gain, up_proj, down_proj, expert_ids, gate_weights):
    members = lax.axis_size("expert")
    per_group = members // EXPERTS
    tokens = hidden_in[0]
    gain = norm_gain[0]
    up_block = up_proj[0]
    down_block = down_proj[0]
    routes = expert_ids[0]
    weights = gate_weights[0]
    rows_here, width = tokens.shape
    top = routes.shape[1]
    square = jnp.mean(tokens.astype(jnp.float32) ** 2, axis=-1, keepdims=True)
    normed = (
        tokens.astype(jnp.float32) * lax.rsqrt(square + 1e-06) * gain.astype(jnp.float32)
    ).astype(jnp.bfloat16)
    chosen = routes[:, :, None] == jnp.arange(EXPERTS)[None, None, :]
    named = jnp.sum(chosen.astype(jnp.int32), axis=1)
    positions = jnp.arange(rows_here)
    earlier = (positions[None, :] < positions[:, None]).astype(jnp.int32)
    before = jnp.dot(earlier, named, preferred_element_type=jnp.int32)
    rank = jnp.sum(jnp.where(chosen, before[:, None, :], 0), axis=2)
    slot = jnp.arange(members * CAP)
    slot_device = slot % members
    slot_rank = slot // members
    slot_expert = slot_device // per_group
    hits = (routes[None, :, :] == slot_expert[:, None, None]) & (rank[None, :, :] == slot_rank[:, None, None])
    picker = jnp.any(hits, axis=2).astype(jnp.bfloat16)
    outgoing = jnp.dot(picker, normed, preferred_element_type=jnp.float32).astype(jnp.bfloat16)
    outgoing = outgoing.reshape(CAP, members, width).transpose(1, 0, 2).reshape(members, -1, LANES)
    incoming = lax.all_to_all(outgoing, "expert", split_axis=0, concat_axis=0, tiled=True)
    incoming = incoming.reshape(members, CAP, width)
    inner = jnp.einsum("spd,fd->spf", incoming, up_block, preferred_element_type=jnp.float32)
    active = jax.nn.silu(inner).astype(jnp.bfloat16)
    partial = jnp.einsum("spf,fd->spd", active, down_block, preferred_element_type=jnp.float32).astype(jnp.bfloat16)
    returned = lax.all_to_all(partial.reshape(members, -1, LANES), "expert", split_axis=0, concat_axis=0, tiled=True)
    returned = returned.reshape(members, CAP, width).transpose(1, 0, 2)
    combine = jnp.sum(jnp.where(hits, weights[None, :, :], 0.0), axis=2).T.reshape(rows_here, CAP, members)
    combine_hi = combine.astype(jnp.bfloat16)
    combine_lo = (combine - combine_hi.astype(jnp.float32)).astype(jnp.bfloat16)
    mixture = jnp.einsum("rps,psd->rd", combine_hi, returned, preferred_element_type=jnp.float32)
    mixture = mixture + jnp.einsum("rps,psd->rd", combine_lo, returned, preferred_element_type=jnp.float32)
    section_out = (tokens.astype(jnp.float32) + mixture).astype(jnp.bfloat16)
    handed = passed_along(section_out, "segment", 1)
    return handed[None]


def solution(mesh):
    in_specs = (
        P("segment", "expert", None),
        P("segment", None),
        P("segment", "expert", None),
        P("segment", "expert", None),
        P("segment", "expert", None),
        P("segment", "expert", None),
    )
    out_specs = P("segment", "expert", None)
    return jax.shard_map(shards, mesh=mesh, in_specs=in_specs, out_specs=out_specs, check_vma=False)
```

```python
import jax
import jax.numpy as jnp
from jax import lax
from jax.sharding import PartitionSpec as P

EXPERTS = 8
CAP = 7
SLOTS = 8


def passed_along(shard, axis, by):
    count = lax.axis_size(axis)
    return lax.ppermute(shard, axis, [(i, (i + by) % count) for i in range(count)])


def shards(hidden_in, norm_gain, up_proj, down_proj, expert_ids, gate_weights):
    members = lax.axis_size("expert")
    per_group = members // EXPERTS
    tokens = hidden_in[0]
    gain = norm_gain[0]
    up_block = up_proj[0]
    down_block = down_proj[0]
    routes = expert_ids[0]
    weights = gate_weights[0]
    rows_here, width = tokens.shape
    top = routes.shape[1]
    square = jnp.mean(tokens.astype(jnp.float32) ** 2, axis=-1, keepdims=True)
    normed = (
        tokens.astype(jnp.float32) * lax.rsqrt(square + 1e-06) * gain.astype(jnp.float32)
    ).astype(jnp.bfloat16)
    chosen = routes[:, :, None] == jnp.arange(EXPERTS)[None, None, :]
    named = jnp.sum(chosen.astype(jnp.int32), axis=1)
    positions = jnp.arange(rows_here)
    earlier = (positions[None, :] < positions[:, None]).astype(jnp.int32)
    before = jnp.dot(earlier, named, preferred_element_type=jnp.int32)
    rank = jnp.sum(jnp.where(chosen, before[:, None, :], 0), axis=2)
    slot = jnp.arange(members * SLOTS)
    slot_device = slot % members
    slot_rank = slot // members
    slot_expert = slot_device // per_group
    hits = (routes[None, :, :] == slot_expert[:, None, None]) & (rank[None, :, :] == slot_rank[:, None, None])
    picker = jnp.any(hits, axis=2).astype(jnp.bfloat16)
    outgoing = jnp.dot(picker, normed, preferred_element_type=jnp.float32).astype(jnp.bfloat16)
    outgoing = outgoing.reshape(SLOTS, members, width)
    incoming = lax.all_to_all(outgoing, "expert", split_axis=1, concat_axis=1, tiled=True)
    inner = jnp.einsum("psd,fd->psf", incoming, up_block, preferred_element_type=jnp.float32)
    active = jax.nn.silu(inner).astype(jnp.bfloat16)
    partial = jnp.einsum("psf,fd->psd", active, down_block, preferred_element_type=jnp.float32).astype(jnp.bfloat16)
    returned = lax.all_to_all(partial, "expert", split_axis=1, concat_axis=1, tiled=True)
    combine = jnp.sum(jnp.where(hits, weights[None, :, :], 0.0), axis=2).T.reshape(rows_here, SLOTS, members)
    combine_hi = combine.astype(jnp.bfloat16)
    combine_lo = (combine - combine_hi.astype(jnp.float32)).astype(jnp.bfloat16)
    mixture = jnp.einsum("rps,psd->rd", combine_hi, returned, preferred_element_type=jnp.float32)
    mixture = mixture + jnp.einsum("rps,psd->rd", combine_lo, returned, preferred_element_type=jnp.float32)
    section_out = (tokens.astype(jnp.float32) + mixture).astype(jnp.bfloat16)
    handed = passed_along(section_out, "segment", 1)
    return handed[None]


def solution(mesh):
    in_specs = (
        P("segment", "expert", None),
        P("segment", None),
        P("segment", "expert", None),
        P("segment", "expert", None),
        P("segment", "expert", None),
        P("segment", "expert", None),
    )
    out_specs = P("segment", "expert", None)
    return jax.shard_map(shards, mesh=mesh, in_specs=in_specs, out_specs=out_specs, check_vma=False)
```

```python
import jax
import jax.numpy as jnp
from jax import lax
from jax.sharding import PartitionSpec as P

EXPERTS = 8
CAP = 7
SLOTS = 8


def passed_along(shard, axis, by):
    count = lax.axis_size(axis)
    return lax.ppermute(shard, axis, [(i, (i + by) % count) for i in range(count)])


def shards(hidden_in, norm_gain, up_proj, down_proj, expert_ids, gate_weights):
    members = lax.axis_size("expert")
    per_group = members // EXPERTS
    tokens = hidden_in[0]
    gain = norm_gain[0]
    up_block = up_proj[0]
    down_block = down_proj[0]
    routes = expert_ids[0]
    weights = gate_weights[0]
    rows_here, width = tokens.shape
    top = routes.shape[1]
    square = jnp.mean(tokens.astype(jnp.float32) ** 2, axis=-1, keepdims=True)
    normed = (
        tokens.astype(jnp.float32) * lax.rsqrt(square + 1e-06) * gain.astype(jnp.float32)
    ).astype(jnp.bfloat16)
    chosen = routes[:, :, None] == jnp.arange(EXPERTS)[None, None, :]
    named = jnp.sum(chosen.astype(jnp.int32), axis=1)
    positions = jnp.arange(rows_here)
    earlier = (positions[None, :] < positions[:, None]).astype(jnp.int32)
    before = jnp.dot(earlier, named, preferred_element_type=jnp.int32)
    rank = jnp.sum(jnp.where(chosen, before[:, None, :], 0), axis=2)
    slot = jnp.arange(members * SLOTS)
    slot_device = slot // SLOTS
    slot_rank = slot % SLOTS
    slot_expert = slot_device // per_group
    hits = (routes[None, :, :] == slot_expert[:, None, None]) & (rank[None, :, :] == slot_rank[:, None, None])
    picker = jnp.any(hits, axis=2).astype(jnp.bfloat16)
    outgoing = jnp.dot(picker, normed, preferred_element_type=jnp.float32).astype(jnp.bfloat16)
    incoming = lax.all_to_all(outgoing, "expert", split_axis=0, concat_axis=0, tiled=True)
    inner = jnp.dot(incoming, up_block.T, preferred_element_type=jnp.float32)
    active = lax.optimization_barrier(jax.nn.silu(inner).astype(jnp.bfloat16))
    partial = jnp.dot(active, down_block, preferred_element_type=jnp.float32).astype(jnp.bfloat16)
    returned = lax.all_to_all(partial, "expert", split_axis=0, concat_axis=0, tiled=True)
    combine = jnp.sum(jnp.where(hits, weights[None, :, :], 0.0), axis=2).T
    combine_hi = combine.astype(jnp.bfloat16)
    combine_lo = (combine - combine_hi.astype(jnp.float32)).astype(jnp.bfloat16)
    mixture = jnp.einsum("rj,jd->rd", combine_hi, returned, preferred_element_type=jnp.float32)
    mixture = mixture + jnp.einsum("rj,jd->rd", combine_lo, returned, preferred_element_type=jnp.float32)
    section_out = (tokens.astype(jnp.float32) + mixture).astype(jnp.bfloat16)
    handed = passed_along(section_out, "segment", 1)
    return handed[None]


def solution(mesh):
    in_specs = (
        P("segment", "expert", None),
        P("segment", None),
        P("segment", "expert", None),
        P("segment", "expert", None),
        P("segment", "expert", None),
        P("segment", "expert", None),
    )
    out_specs = P("segment", "expert", None)
    return jax.shard_map(shards, mesh=mesh, in_specs=in_specs, out_specs=out_specs, check_vma=False)
```

```python
import jax
import jax.numpy as jnp
from jax import lax
from jax.sharding import PartitionSpec as P
from jax.experimental import pallas as pl
from jax.experimental.pallas import tpu as pltpu

EXPERTS = 8
CAP = 7
SLOTS = 8
CHUNK = 1024


def passed_along(shard, axis, by):
    count = lax.axis_size(axis)
    return lax.ppermute(shard, axis, [(i, (i + by) % count) for i in range(count)])


def up_kernel(rows_ref, weights_ref, out_ref, total_ref):
    step = pl.program_id(0)

    @pl.when(step == 0)
    def _():
        total_ref[...] = jnp.zeros_like(total_ref)

    total_ref[...] += lax.dot_general(
        rows_ref[...], weights_ref[...], (((1,), (1,)), ((), ())), preferred_element_type=jnp.float32
    )

    @pl.when(step == pl.num_programs(0) - 1)
    def _():
        out_ref[...] = jax.nn.silu(total_ref[...]).astype(out_ref.dtype)


def up_projection(rows, weights):
    count, width = rows.shape
    units = weights.shape[0]
    return pl.pallas_call(
        up_kernel,
        grid=(width // CHUNK,),
        in_specs=[
            pl.BlockSpec((count, CHUNK), lambda k: (0, k)),
            pl.BlockSpec((units, CHUNK), lambda k: (0, k)),
        ],
        out_specs=pl.BlockSpec((count, units), lambda k: (0, 0)),
        out_shape=jax.ShapeDtypeStruct((count, units), rows.dtype),
        scratch_shapes=[pltpu.VMEM((count, units), jnp.float32)],
    )(rows, weights)


def down_kernel(active_ref, weights_ref, out_ref):
    out_ref[...] = jnp.dot(active_ref[...], weights_ref[...], preferred_element_type=jnp.float32).astype(out_ref.dtype)


def down_projection(active, weights):
    count, units = active.shape
    width = weights.shape[1]
    return pl.pallas_call(
        down_kernel,
        grid=(width // CHUNK,),
        in_specs=[
            pl.BlockSpec((count, units), lambda n: (0, 0)),
            pl.BlockSpec((units, CHUNK), lambda n: (0, n)),
        ],
        out_specs=pl.BlockSpec((count, CHUNK), lambda n: (0, n)),
        out_shape=jax.ShapeDtypeStruct((count, width), active.dtype),
    )(active, weights)


def shards(hidden_in, norm_gain, up_proj, down_proj, expert_ids, gate_weights):
    members = lax.axis_size("expert")
    per_group = members // EXPERTS
    tokens = hidden_in[0]
    gain = norm_gain[0]
    up_block = up_proj[0]
    down_block = down_proj[0]
    routes = expert_ids[0]
    weights = gate_weights[0]
    rows_here, width = tokens.shape
    top = routes.shape[1]
    square = jnp.mean(tokens.astype(jnp.float32) ** 2, axis=-1, keepdims=True)
    normed = (
        tokens.astype(jnp.float32) * lax.rsqrt(square + 1e-06) * gain.astype(jnp.float32)
    ).astype(jnp.bfloat16)
    chosen = routes[:, :, None] == jnp.arange(EXPERTS)[None, None, :]
    named = jnp.sum(chosen.astype(jnp.int32), axis=1)
    positions = jnp.arange(rows_here)
    earlier = (positions[None, :] < positions[:, None]).astype(jnp.int32)
    before = jnp.dot(earlier, named, preferred_element_type=jnp.int32)
    rank = jnp.sum(jnp.where(chosen, before[:, None, :], 0), axis=2)
    slot = jnp.arange(members * SLOTS)
    slot_device = slot // SLOTS
    slot_rank = slot % SLOTS
    slot_expert = slot_device // per_group
    hits = (routes[None, :, :] == slot_expert[:, None, None]) & (rank[None, :, :] == slot_rank[:, None, None])
    picker = jnp.any(hits, axis=2).astype(jnp.bfloat16)
    outgoing = jnp.dot(picker, normed, preferred_element_type=jnp.float32).astype(jnp.bfloat16)
    incoming = lax.all_to_all(outgoing, "expert", split_axis=0, concat_axis=0, tiled=True)
    active = up_projection(incoming, up_block)
    partial = down_projection(active, down_block)
    returned = lax.all_to_all(partial, "expert", split_axis=0, concat_axis=0, tiled=True)
    combine = jnp.sum(jnp.where(hits, weights[None, :, :], 0.0), axis=2).T
    combine_hi = combine.astype(jnp.bfloat16)
    combine_lo = (combine - combine_hi.astype(jnp.float32)).astype(jnp.bfloat16)
    mixture = jnp.einsum("rj,jd->rd", combine_hi, returned, preferred_element_type=jnp.float32)
    mixture = mixture + jnp.einsum("rj,jd->rd", combine_lo, returned, preferred_element_type=jnp.float32)
    section_out = (tokens.astype(jnp.float32) + mixture).astype(jnp.bfloat16)
    handed = passed_along(section_out, "segment", 1)
    return handed[None]


def solution(mesh):
    in_specs = (
        P("segment", "expert", None),
        P("segment", None),
        P("segment", "expert", None),
        P("segment", "expert", None),
        P("segment", "expert", None),
        P("segment", "expert", None),
    )
    out_specs = P("segment", "expert", None)
    return jax.shard_map(shards, mesh=mesh, in_specs=in_specs, out_specs=out_specs, check_vma=False)
```

```python
import jax
import jax.numpy as jnp
from jax import lax
from jax.sharding import PartitionSpec as P
from jax.experimental import pallas as pl
from jax.experimental.pallas import tpu as pltpu

EXPERTS = 8
CAP = 7
SLOTS = 8
CHUNK = 3584


def passed_along(shard, axis, by):
    count = lax.axis_size(axis)
    return lax.ppermute(shard, axis, [(i, (i + by) % count) for i in range(count)])


def up_kernel(rows_ref, weights_ref, out_ref, total_ref):
    step = pl.program_id(0)

    @pl.when(step == 0)
    def _():
        total_ref[...] = jnp.zeros_like(total_ref)

    total_ref[...] += lax.dot_general(
        rows_ref[...], weights_ref[...], (((1,), (1,)), ((), ())), preferred_element_type=jnp.float32
    )

    @pl.when(step == pl.num_programs(0) - 1)
    def _():
        out_ref[...] = jax.nn.silu(total_ref[...]).astype(out_ref.dtype)


def up_projection(rows, weights):
    count, width = rows.shape
    units = weights.shape[0]
    return pl.pallas_call(
        up_kernel,
        grid=(width // CHUNK,),
        in_specs=[
            pl.BlockSpec((count, CHUNK), lambda k: (0, k)),
            pl.BlockSpec((units, CHUNK), lambda k: (0, k)),
        ],
        out_specs=pl.BlockSpec((count, units), lambda k: (0, 0)),
        out_shape=jax.ShapeDtypeStruct((count, units), rows.dtype),
        scratch_shapes=[pltpu.VMEM((count, units), jnp.float32)],
    )(rows, weights)


def down_kernel(active_ref, weights_ref, out_ref):
    out_ref[...] = jnp.dot(active_ref[...], weights_ref[...], preferred_element_type=jnp.float32).astype(out_ref.dtype)


def down_projection(active, weights):
    count, units = active.shape
    width = weights.shape[1]
    return pl.pallas_call(
        down_kernel,
        grid=(width // CHUNK,),
        in_specs=[
            pl.BlockSpec((count, units), lambda n: (0, 0)),
            pl.BlockSpec((units, CHUNK), lambda n: (0, n)),
        ],
        out_specs=pl.BlockSpec((count, CHUNK), lambda n: (0, n)),
        out_shape=jax.ShapeDtypeStruct((count, width), active.dtype),
    )(active, weights)


def shards(hidden_in, norm_gain, up_proj, down_proj, expert_ids, gate_weights):
    members = lax.axis_size("expert")
    per_group = members // EXPERTS
    tokens = hidden_in[0]
    gain = norm_gain[0]
    up_block = up_proj[0]
    down_block = down_proj[0]
    routes = expert_ids[0]
    weights = gate_weights[0]
    rows_here, width = tokens.shape
    top = routes.shape[1]
    square = jnp.mean(tokens.astype(jnp.float32) ** 2, axis=-1, keepdims=True)
    normed = (
        tokens.astype(jnp.float32) * lax.rsqrt(square + 1e-06) * gain.astype(jnp.float32)
    ).astype(jnp.bfloat16)
    chosen = routes[:, :, None] == jnp.arange(EXPERTS)[None, None, :]
    named = jnp.sum(chosen.astype(jnp.int32), axis=1)
    positions = jnp.arange(rows_here)
    earlier = (positions[None, :] < positions[:, None]).astype(jnp.int32)
    before = jnp.dot(earlier, named, preferred_element_type=jnp.int32)
    rank = jnp.sum(jnp.where(chosen, before[:, None, :], 0), axis=2)
    slot = jnp.arange(members * SLOTS)
    slot_device = slot // SLOTS
    slot_rank = slot % SLOTS
    slot_expert = slot_device // per_group
    hits = (routes[None, :, :] == slot_expert[:, None, None]) & (rank[None, :, :] == slot_rank[:, None, None])
    picker = jnp.any(hits, axis=2).astype(jnp.bfloat16)
    outgoing = jnp.dot(picker, normed, preferred_element_type=jnp.float32).astype(jnp.bfloat16)
    incoming = lax.all_to_all(outgoing, "expert", split_axis=0, concat_axis=0, tiled=True)
    active = up_projection(incoming, up_block)
    partial = down_projection(active, down_block)
    returned = lax.all_to_all(partial, "expert", split_axis=0, concat_axis=0, tiled=True)
    combine = jnp.sum(jnp.where(hits, weights[None, :, :], 0.0), axis=2).T
    combine_hi = combine.astype(jnp.bfloat16)
    combine_lo = (combine - combine_hi.astype(jnp.float32)).astype(jnp.bfloat16)
    mixture = jnp.einsum("rj,jd->rd", combine_hi, returned, preferred_element_type=jnp.float32)
    mixture = mixture + jnp.einsum("rj,jd->rd", combine_lo, returned, preferred_element_type=jnp.float32)
    section_out = (tokens.astype(jnp.float32) + mixture).astype(jnp.bfloat16)
    handed = passed_along(section_out, "segment", 1)
    return handed[None]


def solution(mesh):
    in_specs = (
        P("segment", "expert", None),
        P("segment", None),
        P("segment", "expert", None),
        P("segment", "expert", None),
        P("segment", "expert", None),
        P("segment", "expert", None),
    )
    out_specs = P("segment", "expert", None)
    return jax.shard_map(shards, mesh=mesh, in_specs=in_specs, out_specs=out_specs, check_vma=False)
```

```python
import jax
import jax.numpy as jnp
from jax import lax
from jax.sharding import PartitionSpec as P

EXPERTS = 8
CAP = 7
SLOTS = 8


def passed_along(shard, axis, by):
    count = lax.axis_size(axis)
    return lax.ppermute(shard, axis, [(i, (i + by) % count) for i in range(count)])


def shards(hidden_in, norm_gain, up_proj, down_proj, expert_ids, gate_weights):
    members = lax.axis_size("expert")
    per_group = members // EXPERTS
    tokens = hidden_in[0]
    gain = norm_gain[0]
    up_block = up_proj[0]
    down_block = down_proj[0]
    routes = expert_ids[0]
    weights = gate_weights[0]
    rows_here, width = tokens.shape
    top = routes.shape[1]
    square = jnp.mean(tokens.astype(jnp.float32) ** 2, axis=-1, keepdims=True)
    normed = (
        tokens.astype(jnp.float32) * lax.rsqrt(square + 1e-06) * gain.astype(jnp.float32)
    ).astype(jnp.bfloat16)
    chosen = routes[:, :, None] == jnp.arange(EXPERTS)[None, None, :]
    named = jnp.sum(chosen.astype(jnp.int32), axis=1)
    positions = jnp.arange(rows_here)
    earlier = (positions[None, :] < positions[:, None]).astype(jnp.int32)
    before = jnp.dot(earlier, named, preferred_element_type=jnp.int32)
    rank = jnp.sum(jnp.where(chosen, before[:, None, :], 0), axis=2)
    slot = jnp.arange(members * SLOTS)
    slot_device = slot % members
    slot_rank = slot // members
    slot_expert = slot_device // per_group
    hits = (routes[None, :, :] == slot_expert[:, None, None]) & (rank[None, :, :] == slot_rank[:, None, None])
    picker = jnp.any(hits, axis=2).astype(jnp.bfloat16)
    outgoing = jnp.dot(picker, normed, preferred_element_type=jnp.float32).astype(jnp.bfloat16)
    outgoing = outgoing.reshape(SLOTS, members, width)
    incoming = lax.all_to_all(outgoing, "expert", split_axis=1, concat_axis=1, tiled=True)
    inner = jnp.einsum("psd,fd->psf", incoming, up_block, preferred_element_type=jnp.float32)
    active = jax.nn.silu(inner).astype(jnp.bfloat16)
    active = lax.optimization_barrier(active.transpose(1, 0, 2).reshape(members * SLOTS, -1))
    partial = jnp.dot(active, down_block, preferred_element_type=jnp.float32).astype(jnp.bfloat16)
    partial = partial.reshape(members, SLOTS, width)
    returned = lax.all_to_all(partial, "expert", split_axis=0, concat_axis=0, tiled=True).transpose(1, 0, 2)
    combine = jnp.sum(jnp.where(hits, weights[None, :, :], 0.0), axis=2).T.reshape(rows_here, SLOTS, members)
    combine_hi = combine.astype(jnp.bfloat16)
    combine_lo = (combine - combine_hi.astype(jnp.float32)).astype(jnp.bfloat16)
    mixture = jnp.einsum("rps,psd->rd", combine_hi, returned, preferred_element_type=jnp.float32)
    mixture = mixture + jnp.einsum("rps,psd->rd", combine_lo, returned, preferred_element_type=jnp.float32)
    section_out = (tokens.astype(jnp.float32) + mixture).astype(jnp.bfloat16)
    handed = passed_along(section_out, "segment", 1)
    return handed[None]


def solution(mesh):
    in_specs = (
        P("segment", "expert", None),
        P("segment", None),
        P("segment", "expert", None),
        P("segment", "expert", None),
        P("segment", "expert", None),
        P("segment", "expert", None),
    )
    out_specs = P("segment", "expert", None)
    return jax.shard_map(shards, mesh=mesh, in_specs=in_specs, out_specs=out_specs, check_vma=False)
```

```python
import jax
import jax.numpy as jnp
from jax import lax
from jax.sharding import PartitionSpec as P

EXPERTS = 8
CAP = 7
SLOTS = 8


def passed_along(shard, axis, by):
    count = lax.axis_size(axis)
    return lax.ppermute(shard, axis, [(i, (i + by) % count) for i in range(count)])


def shards(hidden_in, norm_gain, up_proj, down_proj, expert_ids, gate_weights):
    members = lax.axis_size("expert")
    per_group = members // EXPERTS
    tokens = hidden_in[0]
    gain = norm_gain[0]
    up_block = up_proj[0]
    down_block = down_proj[0]
    routes = expert_ids[0]
    weights = gate_weights[0]
    rows_here, width = tokens.shape
    top = routes.shape[1]
    square = jnp.mean(tokens.astype(jnp.float32) ** 2, axis=-1, keepdims=True)
    normed = (
        tokens.astype(jnp.float32) * lax.rsqrt(square + 1e-06) * gain.astype(jnp.float32)
    ).astype(jnp.bfloat16)
    chosen = routes[:, :, None] == jnp.arange(EXPERTS)[None, None, :]
    named = jnp.sum(chosen.astype(jnp.int32), axis=1)
    positions = jnp.arange(rows_here)
    earlier = (positions[None, :] < positions[:, None]).astype(jnp.int32)
    before = jnp.dot(earlier, named, preferred_element_type=jnp.int32)
    places = jnp.arange(EXPERTS)[None, None, :] * SLOTS + before[:, None, :]
    key = jnp.sum(jnp.where(chosen, places, 0), axis=2)
    slot = jnp.arange(members * SLOTS)
    slot_device = slot % members
    slot_rank = slot // members
    slot_expert = slot_device // per_group
    hits = key[None, :, :] == (slot_expert * SLOTS + slot_rank)[:, None, None]
    picker = jnp.any(hits, axis=2).astype(jnp.bfloat16)
    outgoing = jnp.dot(picker, normed, preferred_element_type=jnp.float32).astype(jnp.bfloat16)
    outgoing = outgoing.reshape(SLOTS, members, width)
    incoming = lax.all_to_all(outgoing, "expert", split_axis=1, concat_axis=1, tiled=True)
    inner = jnp.einsum("psd,fd->psf", incoming, up_block, preferred_element_type=jnp.float32)
    active = jax.nn.silu(inner).astype(jnp.bfloat16)
    active = lax.optimization_barrier(active.transpose(1, 0, 2).reshape(members * SLOTS, -1))
    partial = jnp.dot(active, down_block, preferred_element_type=jnp.float32).astype(jnp.bfloat16)
    partial = partial.reshape(members, SLOTS, width)
    returned = lax.all_to_all(partial, "expert", split_axis=0, concat_axis=0, tiled=True).transpose(1, 0, 2)
    combine = jnp.sum(jnp.where(hits, weights[None, :, :], 0.0), axis=2).T.reshape(rows_here, SLOTS, members)
    combine_hi = combine.astype(jnp.bfloat16)
    combine_lo = (combine - combine_hi.astype(jnp.float32)).astype(jnp.bfloat16)
    mixture = jnp.einsum("rps,psd->rd", combine_hi, returned, preferred_element_type=jnp.float32)
    mixture = mixture + jnp.einsum("rps,psd->rd", combine_lo, returned, preferred_element_type=jnp.float32)
    section_out = (tokens.astype(jnp.float32) + mixture).astype(jnp.bfloat16)
    handed = passed_along(section_out, "segment", 1)
    return handed[None]


def solution(mesh):
    in_specs = (
        P("segment", "expert", None),
        P("segment", None),
        P("segment", "expert", None),
        P("segment", "expert", None),
        P("segment", "expert", None),
        P("segment", "expert", None),
    )
    out_specs = P("segment", "expert", None)
    return jax.shard_map(shards, mesh=mesh, in_specs=in_specs, out_specs=out_specs, check_vma=False)
```

```python
import jax
import jax.numpy as jnp
from jax import lax
from jax.sharding import PartitionSpec as P

EXPERTS = 8
CAP = 7
SLOTS = 8


def passed_along(shard, axis, by):
    count = lax.axis_size(axis)
    return lax.ppermute(shard, axis, [(i, (i + by) % count) for i in range(count)])


def shards(hidden_in, norm_gain, up_proj, down_proj, expert_ids, gate_weights):
    members = lax.axis_size("expert")
    per_group = members // EXPERTS
    tokens = hidden_in[0]
    gain = norm_gain[0]
    up_block = up_proj[0]
    down_block = down_proj[0]
    routes = expert_ids[0]
    weights = gate_weights[0]
    rows_here, width = tokens.shape
    top = routes.shape[1]
    square = jnp.mean(tokens.astype(jnp.float32) ** 2, axis=-1, keepdims=True)
    normed = lax.optimization_barrier((
        tokens.astype(jnp.float32) * lax.rsqrt(square + 1e-06) * gain.astype(jnp.float32)
    ).astype(jnp.bfloat16))
    chosen = routes[:, :, None] == jnp.arange(EXPERTS)[None, None, :]
    named = jnp.sum(chosen.astype(jnp.int32), axis=1)
    positions = jnp.arange(rows_here)
    earlier = (positions[None, :] < positions[:, None]).astype(jnp.int32)
    before = jnp.dot(earlier, named, preferred_element_type=jnp.int32)
    places = jnp.arange(EXPERTS)[None, None, :] * SLOTS + before[:, None, :]
    key = jnp.sum(jnp.where(chosen, places, 0), axis=2)
    slot = jnp.arange(members * SLOTS)
    slot_device = slot % members
    slot_rank = slot // members
    slot_expert = slot_device // per_group
    hits = key[None, :, :] == (slot_expert * SLOTS + slot_rank)[:, None, None]
    picker = jnp.any(hits, axis=2).astype(jnp.bfloat16)
    outgoing = jnp.dot(picker, normed, preferred_element_type=jnp.float32).astype(jnp.bfloat16)
    outgoing = outgoing.reshape(SLOTS, members, width)
    incoming = lax.all_to_all(outgoing, "expert", split_axis=1, concat_axis=1, tiled=True)
    inner = jnp.einsum("psd,fd->psf", incoming, up_block, preferred_element_type=jnp.float32)
    active = jax.nn.silu(inner).astype(jnp.bfloat16)
    active = lax.optimization_barrier(active.transpose(1, 0, 2).reshape(members * SLOTS, -1))
    partial = jnp.dot(active, down_block, preferred_element_type=jnp.float32).astype(jnp.bfloat16)
    partial = partial.reshape(members, SLOTS, width)
    returned = lax.all_to_all(partial, "expert", split_axis=0, concat_axis=0, tiled=True).transpose(1, 0, 2)
    combine = jnp.sum(jnp.where(hits, weights[None, :, :], 0.0), axis=2).T.reshape(rows_here, SLOTS, members)
    combine_hi = combine.astype(jnp.bfloat16)
    combine_lo = (combine - combine_hi.astype(jnp.float32)).astype(jnp.bfloat16)
    mixture = jnp.einsum("rps,psd->rd", combine_hi, returned, preferred_element_type=jnp.float32)
    mixture = mixture + jnp.einsum("rps,psd->rd", combine_lo, returned, preferred_element_type=jnp.float32)
    section_out = (tokens.astype(jnp.float32) + mixture).astype(jnp.bfloat16)
    handed = passed_along(section_out, "segment", 1)
    return handed[None]


def solution(mesh):
    in_specs = (
        P("segment", "expert", None),
        P("segment", None),
        P("segment", "expert", None),
        P("segment", "expert", None),
        P("segment", "expert", None),
        P("segment", "expert", None),
    )
    out_specs = P("segment", "expert", None)
    return jax.shard_map(shards, mesh=mesh, in_specs=in_specs, out_specs=out_specs, check_vma=False)
```

```python
import jax
import jax.numpy as jnp
from jax import lax
from jax.sharding import PartitionSpec as P

EXPERTS = 8
CAP = 7
SLOTS = 8


def passed_along(shard, axis, by):
    count = lax.axis_size(axis)
    return lax.ppermute(shard, axis, [(i, (i + by) % count) for i in range(count)])


def shards(hidden_in, norm_gain, up_proj, down_proj, expert_ids, gate_weights):
    members = lax.axis_size("expert")
    per_group = members // EXPERTS
    tokens = hidden_in[0]
    gain = norm_gain[0]
    up_block = up_proj[0]
    down_block = down_proj[0]
    routes = expert_ids[0]
    weights = gate_weights[0]
    rows_here, width = tokens.shape
    top = routes.shape[1]
    square = jnp.mean(tokens.astype(jnp.float32) ** 2, axis=-1, keepdims=True)
    normed = (
        tokens.astype(jnp.float32) * lax.rsqrt(square + 1e-06) * gain.astype(jnp.float32)
    ).astype(jnp.bfloat16)
    chosen = lax.optimization_barrier((routes[:, :, None] == jnp.arange(EXPERTS)[None, None, :]).astype(jnp.int32))
    named = jnp.sum(chosen, axis=1)
    positions = jnp.arange(rows_here)
    earlier = (positions[None, :] < positions[:, None]).astype(jnp.int32)
    before = jnp.dot(earlier, named, preferred_element_type=jnp.int32)
    places = jnp.arange(EXPERTS)[None, None, :] * SLOTS + before[:, None, :]
    key = jnp.sum(chosen * places, axis=2)
    slot = jnp.arange(members * SLOTS)
    slot_device = slot % members
    slot_rank = slot // members
    slot_expert = slot_device // per_group
    hits = key[None, :, :] == (slot_expert * SLOTS + slot_rank)[:, None, None]
    picker = jnp.any(hits, axis=2).astype(jnp.bfloat16)
    outgoing = jnp.dot(picker, normed, preferred_element_type=jnp.float32).astype(jnp.bfloat16)
    outgoing = outgoing.reshape(SLOTS, members, width)
    incoming = lax.all_to_all(outgoing, "expert", split_axis=1, concat_axis=1, tiled=True)
    inner = jnp.einsum("psd,fd->psf", incoming, up_block, preferred_element_type=jnp.float32)
    active = jax.nn.silu(inner).astype(jnp.bfloat16)
    active = lax.optimization_barrier(active.transpose(1, 0, 2).reshape(members * SLOTS, -1))
    partial = jnp.dot(active, down_block, preferred_element_type=jnp.float32).astype(jnp.bfloat16)
    partial = partial.reshape(members, SLOTS, width)
    returned = lax.all_to_all(partial, "expert", split_axis=0, concat_axis=0, tiled=True).transpose(1, 0, 2)
    combine = jnp.sum(jnp.where(hits, weights[None, :, :], 0.0), axis=2).T.reshape(rows_here, SLOTS, members)
    combine_hi = combine.astype(jnp.bfloat16)
    combine_lo = (combine - combine_hi.astype(jnp.float32)).astype(jnp.bfloat16)
    mixture = jnp.einsum("rps,psd->rd", combine_hi, returned, preferred_element_type=jnp.float32)
    mixture = mixture + jnp.einsum("rps,psd->rd", combine_lo, returned, preferred_element_type=jnp.float32)
    section_out = (tokens.astype(jnp.float32) + mixture).astype(jnp.bfloat16)
    handed = passed_along(section_out, "segment", 1)
    return handed[None]


def solution(mesh):
    in_specs = (
        P("segment", "expert", None),
        P("segment", None),
        P("segment", "expert", None),
        P("segment", "expert", None),
        P("segment", "expert", None),
        P("segment", "expert", None),
    )
    out_specs = P("segment", "expert", None)
    return jax.shard_map(shards, mesh=mesh, in_specs=in_specs, out_specs=out_specs, check_vma=False)
```

```python
import jax
import jax.numpy as jnp
from jax import lax
from jax.sharding import PartitionSpec as P

EXPERTS = 8
CAP = 7
SLOTS = 8


def passed_along(shard, axis, by):
    count = lax.axis_size(axis)
    return lax.ppermute(shard, axis, [(i, (i + by) % count) for i in range(count)])


def shards(hidden_in, norm_gain, up_proj, down_proj, expert_ids, gate_weights):
    members = lax.axis_size("expert")
    per_group = members // EXPERTS
    tokens = hidden_in[0]
    gain = norm_gain[0]
    up_block = up_proj[0]
    down_block = down_proj[0]
    routes = expert_ids[0]
    weights = gate_weights[0]
    rows_here, width = tokens.shape
    top = routes.shape[1]
    wide = lax.optimization_barrier(tokens.astype(jnp.float32))
    square = jnp.mean(wide ** 2, axis=-1, keepdims=True)
    normed = (wide * lax.rsqrt(square + 1e-06) * gain.astype(jnp.float32)).astype(jnp.bfloat16)
    chosen = lax.optimization_barrier((routes[:, :, None] == jnp.arange(EXPERTS)[None, None, :]).astype(jnp.int32))
    named = jnp.sum(chosen, axis=1)
    positions = jnp.arange(rows_here)
    earlier = (positions[None, :] < positions[:, None]).astype(jnp.int32)
    before = jnp.dot(earlier, named, preferred_element_type=jnp.int32)
    places = jnp.arange(EXPERTS)[None, None, :] * SLOTS + before[:, None, :]
    key = jnp.sum(chosen * places, axis=2)
    slot = jnp.arange(members * SLOTS)
    slot_device = slot % members
    slot_rank = slot // members
    slot_expert = slot_device // per_group
    hits = key[None, :, :] == (slot_expert * SLOTS + slot_rank)[:, None, None]
    picker = jnp.any(hits, axis=2).astype(jnp.bfloat16)
    outgoing = jnp.dot(picker, normed, preferred_element_type=jnp.float32).astype(jnp.bfloat16)
    outgoing = outgoing.reshape(SLOTS, members, width)
    incoming = lax.all_to_all(outgoing, "expert", split_axis=1, concat_axis=1, tiled=True)
    inner = jnp.einsum("psd,fd->psf", incoming, up_block, preferred_element_type=jnp.float32)
    active = jax.nn.silu(inner).astype(jnp.bfloat16)
    active = lax.optimization_barrier(active.transpose(1, 0, 2).reshape(members * SLOTS, -1))
    partial = jnp.dot(active, down_block, preferred_element_type=jnp.float32).astype(jnp.bfloat16)
    partial = partial.reshape(members, SLOTS, width)
    returned = lax.all_to_all(partial, "expert", split_axis=0, concat_axis=0, tiled=True).transpose(1, 0, 2)
    combine = jnp.sum(jnp.where(hits, weights[None, :, :], 0.0), axis=2).T.reshape(rows_here, SLOTS, members)
    combine_hi = combine.astype(jnp.bfloat16)
    combine_lo = (combine - combine_hi.astype(jnp.float32)).astype(jnp.bfloat16)
    mixture = jnp.einsum("rps,psd->rd", combine_hi, returned, preferred_element_type=jnp.float32)
    mixture = mixture + jnp.einsum("rps,psd->rd", combine_lo, returned, preferred_element_type=jnp.float32)
    section_out = (tokens.astype(jnp.float32) + mixture).astype(jnp.bfloat16)
    handed = passed_along(section_out, "segment", 1)
    return handed[None]


def solution(mesh):
    in_specs = (
        P("segment", "expert", None),
        P("segment", None),
        P("segment", "expert", None),
        P("segment", "expert", None),
        P("segment", "expert", None),
        P("segment", "expert", None),
    )
    out_specs = P("segment", "expert", None)
    return jax.shard_map(shards, mesh=mesh, in_specs=in_specs, out_specs=out_specs, check_vma=False)
```

```python
import jax
import jax.numpy as jnp
from jax import lax
from jax.sharding import PartitionSpec as P

EXPERTS = 8
CAP = 7
SLOTS = 8


def passed_along(shard, axis, by):
    count = lax.axis_size(axis)
    return lax.ppermute(shard, axis, [(i, (i + by) % count) for i in range(count)])


def shards(hidden_in, norm_gain, up_proj, down_proj, expert_ids, gate_weights):
    members = lax.axis_size("expert")
    per_group = members // EXPERTS
    tokens = hidden_in[0]
    gain = norm_gain[0]
    up_block = up_proj[0]
    down_block = down_proj[0]
    routes = expert_ids[0]
    weights = gate_weights[0]
    rows_here, width = tokens.shape
    top = routes.shape[1]
    stacked = lax.optimization_barrier(jnp.concatenate([tokens, gain[None, :]], axis=0).astype(jnp.float32))
    wide = stacked[:rows_here]
    square = jnp.mean(wide ** 2, axis=-1, keepdims=True)
    normed = (wide * lax.rsqrt(square + 1e-06) * stacked[rows_here:]).astype(jnp.bfloat16)
    chosen = lax.optimization_barrier((routes[:, :, None] == jnp.arange(EXPERTS)[None, None, :]).astype(jnp.int32))
    named = jnp.sum(chosen, axis=1)
    positions = jnp.arange(rows_here)
    earlier = (positions[None, :] < positions[:, None]).astype(jnp.int32)
    before = jnp.dot(earlier, named, preferred_element_type=jnp.int32)
    places = jnp.arange(EXPERTS)[None, None, :] * SLOTS + before[:, None, :]
    key = jnp.sum(chosen * places, axis=2)
    slot = jnp.arange(members * SLOTS)
    slot_device = slot % members
    slot_rank = slot // members
    slot_expert = slot_device // per_group
    hits = key[None, :, :] == (slot_expert * SLOTS + slot_rank)[:, None, None]
    picker = jnp.any(hits, axis=2).astype(jnp.bfloat16)
    outgoing = jnp.dot(picker, normed, preferred_element_type=jnp.float32).astype(jnp.bfloat16)
    outgoing = outgoing.reshape(SLOTS, members, width)
    incoming = lax.all_to_all(outgoing, "expert", split_axis=1, concat_axis=1, tiled=True)
    inner = jnp.einsum("psd,fd->psf", incoming, up_block, preferred_element_type=jnp.float32)
    active = jax.nn.silu(inner).astype(jnp.bfloat16)
    active = lax.optimization_barrier(active.transpose(1, 0, 2).reshape(members * SLOTS, -1))
    partial = jnp.dot(active, down_block, preferred_element_type=jnp.float32).astype(jnp.bfloat16)
    partial = partial.reshape(members, SLOTS, width)
    returned = lax.all_to_all(partial, "expert", split_axis=0, concat_axis=0, tiled=True).transpose(1, 0, 2)
    combine = jnp.sum(jnp.where(hits, weights[None, :, :], 0.0), axis=2).T.reshape(rows_here, SLOTS, members)
    combine_hi = combine.astype(jnp.bfloat16)
    combine_lo = (combine - combine_hi.astype(jnp.float32)).astype(jnp.bfloat16)
    mixture = jnp.einsum("rps,psd->rd", combine_hi, returned, preferred_element_type=jnp.float32)
    mixture = mixture + jnp.einsum("rps,psd->rd", combine_lo, returned, preferred_element_type=jnp.float32)
    section_out = (tokens.astype(jnp.float32) + mixture).astype(jnp.bfloat16)
    handed = passed_along(section_out, "segment", 1)
    return handed[None]


def solution(mesh):
    in_specs = (
        P("segment", "expert", None),
        P("segment", None),
        P("segment", "expert", None),
        P("segment", "expert", None),
        P("segment", "expert", None),
        P("segment", "expert", None),
    )
    out_specs = P("segment", "expert", None)
    return jax.shard_map(shards, mesh=mesh, in_specs=in_specs, out_specs=out_specs, check_vma=False)
```

```python
import jax
import jax.numpy as jnp
from jax import lax
from jax.sharding import PartitionSpec as P

EXPERTS = 8
CAP = 7
SLOTS = 8


def passed_along(shard, axis, by):
    count = lax.axis_size(axis)
    return lax.ppermute(shard, axis, [(i, (i + by) % count) for i in range(count)])


def shards(hidden_in, norm_gain, up_proj, down_proj, expert_ids, gate_weights):
    members = lax.axis_size("expert")
    per_group = members // EXPERTS
    tokens = hidden_in[0]
    gain = norm_gain[0]
    up_block = up_proj[0]
    down_block = down_proj[0]
    routes = expert_ids[0]
    weights = gate_weights[0]
    rows_here, width = tokens.shape
    top = routes.shape[1]
    stacked = lax.optimization_barrier(jnp.concatenate([tokens, gain[None, :]], axis=0).astype(jnp.float32))
    wide = stacked[:rows_here]
    square = jnp.mean(wide ** 2, axis=-1, keepdims=True)
    normed = (wide * lax.rsqrt(square + 1e-06) * stacked[rows_here:]).astype(jnp.bfloat16)
    chosen = lax.optimization_barrier((routes[:, :, None] == jnp.arange(EXPERTS)[None, None, :]).astype(jnp.int32))
    named = jnp.sum(chosen, axis=1)
    positions = jnp.arange(rows_here)
    earlier = (positions[None, :] < positions[:, None]).astype(jnp.int32)
    before = jnp.dot(earlier, named, preferred_element_type=jnp.int32)
    places = jnp.arange(EXPERTS)[None, None, :] * SLOTS + before[:, None, :]
    key = jnp.sum(chosen * places, axis=2)
    slot = jnp.arange(members * SLOTS)
    slot_device = slot % members
    slot_rank = slot // members
    slot_expert = slot_device // per_group
    hits = key[None, :, :] == (slot_expert * SLOTS + slot_rank)[:, None, None]
    picker = jnp.any(hits, axis=2).astype(jnp.bfloat16)
    outgoing = jnp.dot(picker, normed, preferred_element_type=jnp.float32).astype(jnp.bfloat16)
    outgoing = outgoing.reshape(SLOTS, members, width)
    incoming = lax.all_to_all(outgoing, "expert", split_axis=1, concat_axis=1, tiled=True)
    inner = jnp.einsum("psd,fd->psf", incoming, up_block, preferred_element_type=jnp.float32)
    active = jax.nn.silu(inner).astype(jnp.bfloat16)
    active = lax.optimization_barrier(active.transpose(1, 0, 2).reshape(members * SLOTS, -1))
    partial = jnp.dot(active, down_block, preferred_element_type=jnp.float32).astype(jnp.bfloat16)
    partial = partial.reshape(members, SLOTS, width)
    returned = lax.all_to_all(partial, "expert", split_axis=0, concat_axis=0, tiled=True).transpose(1, 0, 2)
    combine = jnp.sum(jnp.where(hits, weights[None, :, :], 0.0), axis=2).T.reshape(rows_here, SLOTS, members)
    combine_hi = combine.astype(jnp.bfloat16)
    combine_lo = (combine - combine_hi.astype(jnp.float32)).astype(jnp.bfloat16)
    both = jnp.concatenate([combine_hi, combine_lo], axis=0)
    mixed = jnp.einsum("rps,psd->rd", both, returned, preferred_element_type=jnp.float32)
    mixture = mixed[:rows_here] + mixed[rows_here:]
    section_out = (tokens.astype(jnp.float32) + mixture).astype(jnp.bfloat16)
    handed = passed_along(section_out, "segment", 1)
    return handed[None]


def solution(mesh):
    in_specs = (
        P("segment", "expert", None),
        P("segment", None),
        P("segment", "expert", None),
        P("segment", "expert", None),
        P("segment", "expert", None),
        P("segment", "expert", None),
    )
    out_specs = P("segment", "expert", None)
    return jax.shard_map(shards, mesh=mesh, in_specs=in_specs, out_specs=out_specs, check_vma=False)
```

```python
import jax
import jax.numpy as jnp
from jax import lax
from jax.sharding import PartitionSpec as P

EXPERTS = 8
CAP = 7
SLOTS = 8


def passed_along(shard, axis, by):
    count = lax.axis_size(axis)
    return lax.ppermute(shard, axis, [(i, (i + by) % count) for i in range(count)])


def shards(hidden_in, norm_gain, up_proj, down_proj, expert_ids, gate_weights):
    members = lax.axis_size("expert")
    per_group = members // EXPERTS
    tokens = hidden_in[0]
    gain = norm_gain[0]
    up_block = up_proj[0]
    down_block = down_proj[0]
    routes = expert_ids[0]
    weights = gate_weights[0]
    rows_here, width = tokens.shape
    top = routes.shape[1]
    stacked, chosen = lax.optimization_barrier((
        jnp.concatenate([tokens, gain[None, :]], axis=0).astype(jnp.float32),
        (routes[:, :, None] == jnp.arange(EXPERTS)[None, None, :]).astype(jnp.int32),
    ))
    wide = stacked[:rows_here]
    square = jnp.mean(wide ** 2, axis=-1, keepdims=True)
    normed = (wide * lax.rsqrt(square + 1e-06) * stacked[rows_here:]).astype(jnp.bfloat16)
    named = jnp.sum(chosen, axis=1)
    positions = jnp.arange(rows_here)
    earlier = (positions[None, :] < positions[:, None]).astype(jnp.int32)
    before = jnp.dot(earlier, named, preferred_element_type=jnp.int32)
    places = jnp.arange(EXPERTS)[None, None, :] * SLOTS + before[:, None, :]
    key = jnp.sum(chosen * places, axis=2)
    slot = jnp.arange(members * SLOTS)
    slot_device = slot % members
    slot_rank = slot // members
    slot_expert = slot_device // per_group
    hits = key[None, :, :] == (slot_expert * SLOTS + slot_rank)[:, None, None]
    picker = jnp.any(hits, axis=2).astype(jnp.bfloat16)
    outgoing = jnp.dot(picker, normed, preferred_element_type=jnp.float32).astype(jnp.bfloat16)
    outgoing = outgoing.reshape(SLOTS, members, width)
    incoming = lax.all_to_all(outgoing, "expert", split_axis=1, concat_axis=1, tiled=True)
    inner = jnp.einsum("psd,fd->psf", incoming, up_block, preferred_element_type=jnp.float32)
    active = jax.nn.silu(inner).astype(jnp.bfloat16)
    active = lax.optimization_barrier(active.transpose(1, 0, 2).reshape(members * SLOTS, -1))
    partial = jnp.dot(active, down_block, preferred_element_type=jnp.float32).astype(jnp.bfloat16)
    partial = partial.reshape(members, SLOTS, width)
    returned = lax.all_to_all(partial, "expert", split_axis=0, concat_axis=0, tiled=True).transpose(1, 0, 2)
    combine = jnp.sum(jnp.where(hits, weights[None, :, :], 0.0), axis=2).T.reshape(rows_here, SLOTS, members)
    combine_hi = combine.astype(jnp.bfloat16)
    combine_lo = (combine - combine_hi.astype(jnp.float32)).astype(jnp.bfloat16)
    mixture = jnp.einsum("rps,psd->rd", combine_hi, returned, preferred_element_type=jnp.float32)
    mixture = mixture + jnp.einsum("rps,psd->rd", combine_lo, returned, preferred_element_type=jnp.float32)
    section_out = (tokens.astype(jnp.float32) + mixture).astype(jnp.bfloat16)
    handed = passed_along(section_out, "segment", 1)
    return handed[None]


def solution(mesh):
    in_specs = (
        P("segment", "expert", None),
        P("segment", None),
        P("segment", "expert", None),
        P("segment", "expert", None),
        P("segment", "expert", None),
        P("segment", "expert", None),
    )
    out_specs = P("segment", "expert", None)
    return jax.shard_map(shards, mesh=mesh, in_specs=in_specs, out_specs=out_specs, check_vma=False)
```
